256 devices in a mesh: band: 16 (over z, x_hi), domain: 16 (over y, x_lo, core).
Axes of the slice: x: 4 (x_hi: 2, x_lo: 2; x = x_hi * 2 + x_lo), y: 4, z: 8, core: 2. Of those that a mesh axis runs over, the one named last changes fastest.
Arguments:
- orbitals: float32 [256, 16384], P('band', 'domain'), may hold values from -12 to 12
- potential: float32 [16384], P('domain'), may hold values from -9 to 4.5
- stencil: int32 [36, 16384], P(None, 'domain'), may hold values from 0 to 1536, as said below
- send_list: int32 [2, 4096], P(None, 'domain'), may hold values from 0 to 1023, as said below
- send_count: int32 [2, 16], P(None, 'domain'), may hold values from 0 to 256, as said below
Outputs:
- filtered: float32 [256, 16384], P('band', 'domain')
- correlation: float32 [256, 256], P('band', 'domain')
- subspace: float32 [256, 256], P('band', 'domain')
The draws below stay inside these ranges and needn't reach their ends.
Inputs may be any that keep to these rules, and one draw needn't show every extreme that they name: `stencil`: entries below 1024 name a slot of the point's own subdomain; entries from 1024 on name only live boundary rows of an existing neighbouring subdomain; 1536 marks a neighbour outside the cluster. `send_list`: each list of 256 entries holds distinct slots of the sending subdomain. `send_count`: row 0 counts the rows subdomain d sends to d + 1, row 1 those it sends to d - 1; zero toward a missing neighbour; 256 is reached in every draw.
All inputs are finite; a program needn't handle non-finite values.
Results may differ from the reference program's by a relative error of at most 0.00015.
Values sent between devices are 32-bit elements; how exact they have to be, the bound alone decides.
No kernel may reach another device: no remote copies, remote signals or barrier semaphores. Data moves between devices by JAX's collectives and lax.ppermute only.
A program may use at most 128 MiB of HBM per device.

```python
import jax
import jax.numpy as jnp
from jax import lax

ORBS = 256
PTS = 1024
NB = 36
DEGREE = 4
CAP = 256
NPTS = 16384
N_DOMAIN = 16


def count_table(key):
    domains = NPTS // PTS
    inner_key = jax.random.fold_in(key, 101)
    first_key, second_key = jax.random.split(inner_key)
    face_index = jnp.arange(domains, dtype=jnp.int32)
    offset = 2 * face_index + 2 - domains
    weight = domains * domains - offset * offset
    middle = domains // 2 - 1
    upward = weight * jax.random.randint(first_key, (domains,), CAP // 2, CAP + 1) // (domains * domains)
    downward = weight * jax.random.randint(second_key, (domains,), CAP // 2, CAP + 1) // (domains * domains)
    upward = jnp.where(face_index == middle, CAP, upward)
    downward = jnp.where(face_index == middle, CAP, downward)
    upward = jnp.where(face_index < domains - 1, upward, 0)
    down_shifted = jnp.concatenate([jnp.zeros((1,), jnp.int32), downward[:-1].astype(jnp.int32)])
    return jnp.stack([upward.astype(jnp.int32), down_shifted]).astype(jnp.int32)


def draw_send_count(key, part):
    return count_table(key)


def draw_stencil(key, part):
    counts = count_table(key)
    below = jnp.concatenate([jnp.zeros((1,), jnp.int32), counts[0, :-1]])
    above = jnp.concatenate([counts[1, 1:], jnp.zeros((1,), jnp.int32)])
    owner_index = jnp.arange(NPTS, dtype=jnp.int32) // PTS
    below_point = below[owner_index][None, :]
    above_point = above[owner_index][None, :]
    inner_key = jax.random.fold_in(key, 202)
    kind_key, local_key, low_key, high_key = jax.random.split(inner_key, 4)
    category = jax.random.randint(kind_key, (NB, NPTS), 0, 100)
    local_slot = jax.random.randint(local_key, (NB, NPTS), 0, PTS)
    low_slot = jax.random.randint(low_key, (NB, NPTS), 0, jnp.maximum(below_point, 1))
    high_slot = jax.random.randint(high_key, (NB, NPTS), 0, jnp.maximum(above_point, 1))
    result = local_slot
    result = jnp.where((category >= 76) & (category < 88) & (below_point > 0), PTS + low_slot, result)
    result = jnp.where((category >= 88) & (category < 98) & (above_point > 0), PTS + CAP + high_slot, result)
    result = jnp.where(category >= 98, PTS + 2 * CAP, result)
    return result.astype(jnp.int32)


def draw_send_list(key, part):
    domains = NPTS // PTS
    list_keys = jax.random.split(jax.random.fold_in(key, 303), 2 * domains)
    chosen = jax.vmap(lambda subkey: jax.random.permutation(subkey, PTS)[:CAP])(list_keys)
    return chosen.reshape(2, domains * CAP).astype(jnp.int32)


def draw_potential(key, part):
    domains = NPTS // PTS
    owner_index = (jnp.arange(NPTS) // PTS).astype(jnp.float32)
    rising = owner_index / max(domains - 1, 1)
    uniform_part = jax.random.uniform(jax.random.fold_in(key, 404), (NPTS,), jnp.float32, -1.0, 0.5)
    domain_scale = 1.0 + 2.0 * rising
    return (domain_scale * uniform_part).astype(jnp.float32)


def draw_orbitals(key, part):
    noise_key, sign_key, level_key = jax.random.split(jax.random.fold_in(key, 505), 3)
    noise_part = jax.random.truncated_normal(noise_key, -4.0, 4.0, (ORBS, NPTS), jnp.float32)
    level = jax.random.uniform(level_key, (ORBS, 1), jnp.float32, 3.0, 5.0)
    sign_pick = jax.random.randint(sign_key, (ORBS, 1), 0, 2)
    signed_level = jnp.where(sign_pick == 0, -level, level)
    return (noise_part + signed_level).astype(jnp.float32)


def setup_inputs(seed: int = 0) -> dict:
    key_list = jax.random.split(jax.random.key(seed), 6)
    return {
        "orbitals": draw_orbitals(jax.random.fold_in(key_list[5], 71), 0),
        "potential": draw_potential(jax.random.fold_in(key_list[5], 71), 0),
        "stencil": draw_stencil(jax.random.fold_in(key_list[5], 71), 0),
        "send_list": draw_send_list(jax.random.fold_in(key_list[5], 71), 0),
        "send_count": draw_send_count(jax.random.fold_in(key_list[5], 71), 0),
    }


WEIGHTS = (-5369.0 / 1800.0, 12.0 / 7.0, -15.0 / 56.0, 10.0 / 189.0, -1.0 / 112.0, 2.0 / 1925.0, -1.0 / 16632.0)
KINETIC = 50.0 / 9.0
CUT_SHARE = 0.1
SPECTRAL_REACH = KINETIC * 3.0 * (abs(WEIGHTS[0]) + 2.0 * (abs(WEIGHTS[1]) + abs(WEIGHTS[2]) + abs(WEIGHTS[3]) + abs(WEIGHTS[4]) + abs(WEIGHTS[5]) + abs(WEIGHTS[6])))


def apply_operator(values, potential, stencil, send_list, send_count):
    orb_total = values.shape[0]
    blocks = values.reshape(orb_total, N_DOMAIN, PTS)
    list_blocks = send_list.reshape(2, N_DOMAIN, CAP)
    live_slots = lax.broadcasted_iota(jnp.int32, (2, N_DOMAIN, CAP), 2) < send_count[:, :, None]
    sent_rows = jax.vmap(lambda block_values, chosen_slots: block_values[:, chosen_slots], in_axes=(1, 1), out_axes=1)(blocks, list_blocks)
    sent_rows = jnp.where(jnp.transpose(live_slots, (1, 0, 2))[None], sent_rows, jnp.zeros_like(sent_rows))
    up_rows = sent_rows[:, :, 0]
    down_rows = sent_rows[:, :, 1]
    empty_rows = jnp.zeros((orb_total, 1, CAP), values.dtype)
    from_below = jnp.concatenate([empty_rows, up_rows[:, :-1]], axis=1)
    from_above = jnp.concatenate([down_rows[:, 1:], empty_rows], axis=1)
    zero_column = jnp.zeros((orb_total, N_DOMAIN, 1), values.dtype)
    buffer = jnp.concatenate([blocks, from_below, from_above, zero_column], axis=2)
    stencil_blocks = stencil.reshape(NB, N_DOMAIN, PTS)

    def one_domain(inputs):
        domain_buffer, neighbours, potential_block, own_values = inputs
        near_sum = jnp.zeros_like(own_values)
        for distance in range(6):
            cycle_sum = jnp.zeros_like(own_values)
            for member in range(6):
                cycle_sum = cycle_sum + domain_buffer[:, neighbours[6 * distance + member]]
            near_sum = near_sum + WEIGHTS[distance + 1] * cycle_sum
        return potential_block * own_values - KINETIC * (3.0 * WEIGHTS[0] * own_values + near_sum)

    result = lax.map(one_domain, (jnp.transpose(buffer, (1, 0, 2)), jnp.transpose(stencil_blocks, (1, 0, 2)), potential.reshape(N_DOMAIN, PTS), jnp.transpose(blocks, (1, 0, 2))))
    return jnp.transpose(result, (1, 0, 2)).reshape(orb_total, NPTS)


def filter_block(orbitals, operator_fn, lowest, highest):
    top_bound = highest + SPECTRAL_REACH
    cut_point = lowest + CUT_SHARE * (top_bound - lowest)
    half_width = (top_bound - cut_point) / 2.0
    centre = (top_bound + cut_point) / 2.0
    sigma_now = half_width / (lowest - centre)
    sigma_scale = 2.0 / sigma_now
    previous = orbitals
    current = (sigma_now / half_width) * (operator_fn(orbitals) - centre * orbitals)
    for order_index in range(2, DEGREE + 1):
        sigma_next = 1.0 / (sigma_scale - sigma_now)
        following = (2.0 * sigma_next / half_width) * (operator_fn(current) - centre * current) - (sigma_now * sigma_next) * previous
        previous = current
        current = following
        sigma_now = sigma_next
    return current


def reference(orbitals, potential, stencil, send_list, send_count):
    lowest = jnp.min(potential)
    highest = jnp.max(potential)

    def operator_fn(values):
        return apply_operator(values, potential, stencil, send_list, send_count)

    filtered = filter_block(orbitals, operator_fn, lowest, highest)
    applied = operator_fn(filtered)
    correlation = jnp.dot(filtered, filtered.T, preferred_element_type=jnp.float32, precision=lax.Precision.HIGHEST) / NPTS
    subspace = jnp.dot(filtered, applied.T, preferred_element_type=jnp.float32, precision=lax.Precision.HIGHEST) / NPTS
    return filtered, correlation, subspace
```

```python
import jax
import jax.numpy as jnp
from jax import lax
from jax.sharding import PartitionSpec as P

DEGREE = 4


WEIGHTS = (
    -5369.0 / 1800.0,
    12.0 / 7.0,
    -15.0 / 56.0,
    10.0 / 189.0,
    -1.0 / 112.0,
    2.0 / 1925.0,
    -1.0 / 16632.0,
)
KINETIC = 50.0 / 9.0
CUT_SHARE = 0.1
SPECTRAL_REACH = (
    KINETIC
    * 3.0
    * (
        abs(WEIGHTS[0])
        + 2.0
        * (
            abs(WEIGHTS[1])
            + abs(WEIGHTS[2])
            + abs(WEIGHTS[3])
            + abs(WEIGHTS[4])
            + abs(WEIGHTS[5])
            + abs(WEIGHTS[6])
        )
    )
)


def dense(left, right):
    return lax.dot_general(
        left,
        right,
        (((1,), (0,)), ((), ())),
        precision=lax.Precision.HIGHEST,
        preferred_element_type=jnp.float32,
    )


def stencil_matrix(stencil, rows):
    slots = lax.broadcasted_iota(jnp.int32, (rows, stencil.shape[1]), 0)
    total = jnp.zeros((rows, stencil.shape[1]), jnp.float32)
    for distance in range(6):
        count = jnp.zeros((rows, stencil.shape[1]), jnp.float32)
        for member in range(6):
            count = count + (slots == stencil[6 * distance + member][None, :]).astype(jnp.float32)
        total = total + WEIGHTS[distance + 1] * count
    return total


def selection_matrix(send_list, live_slots, points):
    slots = lax.broadcasted_iota(jnp.int32, (points, send_list.shape[1]), 0)
    down = (slots == send_list[1][None, :]) & live_slots[1][None, :]
    up = (slots == send_list[0][None, :]) & live_slots[0][None, :]
    return jnp.concatenate([down, up], axis=1).astype(jnp.float32)


def apply_operator(values, potential, pick, near_local, near_below, near_above):
    capacity = pick.shape[1] // 2
    count = lax.axis_size("domain")
    outgoing = dense(values, pick)
    forward = [(i, i + 1) for i in range(count - 1)]
    backward = [(i + 1, i) for i in range(count - 1)]
    from_below = lax.ppermute(outgoing[:, capacity:], "domain", forward)
    from_above = lax.ppermute(outgoing[:, :capacity], "domain", backward)
    near_sum = dense(values, near_local) + dense(from_below, near_below) + dense(from_above, near_above)
    return potential * values - KINETIC * (3.0 * WEIGHTS[0] * values + near_sum)


def filter_block(orbitals, operator_fn, lowest, highest):
    top_bound = highest + SPECTRAL_REACH
    cut_point = lowest + CUT_SHARE * (top_bound - lowest)
    half_width = (top_bound - cut_point) / 2.0
    centre = (top_bound + cut_point) / 2.0
    sigma_now = half_width / (lowest - centre)
    sigma_scale = 2.0 / sigma_now
    previous = orbitals
    current = sigma_now / half_width * (operator_fn(orbitals) - centre * orbitals)
    for order_index in range(2, DEGREE + 1):
        sigma_next = 1.0 / (sigma_scale - sigma_now)
        following = (
            2.0 * sigma_next / half_width * (operator_fn(current) - centre * current)
            - sigma_now * sigma_next * previous
        )
        previous = current
        current = following
        sigma_now = sigma_next
    return current


def inner_products(left_block, right_block):
    return lax.dot_general(
        left_block,
        right_block,
        (((1,), (1,)), ((), ())),
        precision=lax.Precision.HIGHEST,
        preferred_element_type=jnp.float32,
    )


def shards(orbitals, potential, stencil, send_list, send_count):
    rows, points = orbitals.shape
    capacity = send_list.shape[1]
    domain_count = lax.axis_size("domain")
    band_count = lax.axis_size("band")
    total_points = points * domain_count
    extremes = lax.pmax(jnp.stack([-jnp.min(potential), jnp.max(potential)]), "domain")
    lowest = -extremes[0]
    highest = extremes[1]
    live_slots = lax.broadcasted_iota(jnp.int32, (2, capacity), 1) < send_count

    pick = selection_matrix(send_list, live_slots, points)
    weight = stencil_matrix(stencil, points + 2 * capacity)
    near_local = weight[:points]
    near_below = weight[points : points + capacity]
    near_above = weight[points + capacity :]

    def operator_fn(values):
        return apply_operator(values, potential, pick, near_local, near_below, near_above)

    filtered = filter_block(orbitals, operator_fn, lowest, highest)
    applied = operator_fn(filtered)
    both = jnp.stack([filtered, applied])
    gathered = lax.all_gather(both, "band", axis=1, tiled=False)
    gathered = gathered.reshape(2, band_count * rows, points)
    parts = jnp.stack(
        [inner_products(filtered, gathered[0]), inner_products(filtered, gathered[1])]
    )
    sums = lax.psum_scatter(parts, "domain", scatter_dimension=2, tiled=True)
    return (filtered, sums[0] / total_points, sums[1] / total_points)


def solution(mesh):
    placed = (
        P("band", "domain"),
        P("domain"),
        P(None, "domain"),
        P(None, "domain"),
        P(None, "domain"),
    )
    return jax.shard_map(
        shards,
        mesh=mesh,
        in_specs=placed,
        out_specs=(P("band", "domain"), P("band", "domain"), P("band", "domain")),
        check_vma=False,
    )
```

```python
import jax
import jax.numpy as jnp
from jax import lax
from jax.sharding import PartitionSpec as P

DEGREE = 4


WEIGHTS = (
    -5369.0 / 1800.0,
    12.0 / 7.0,
    -15.0 / 56.0,
    10.0 / 189.0,
    -1.0 / 112.0,
    2.0 / 1925.0,
    -1.0 / 16632.0,
)
KINETIC = 50.0 / 9.0
CUT_SHARE = 0.1
SPECTRAL_REACH = (
    KINETIC
    * 3.0
    * (
        abs(WEIGHTS[0])
        + 2.0
        * (
            abs(WEIGHTS[1])
            + abs(WEIGHTS[2])
            + abs(WEIGHTS[3])
            + abs(WEIGHTS[4])
            + abs(WEIGHTS[5])
            + abs(WEIGHTS[6])
        )
    )
)


def dense(left, right):
    return lax.dot_general(
        left,
        right,
        (((1,), (0,)), ((), ())),
        precision=lax.Precision.HIGHEST,
        preferred_element_type=jnp.float32,
    )


def stencil_matrix(stencil, rows):
    slots = lax.broadcasted_iota(jnp.int32, (rows, stencil.shape[1]), 0)
    total = jnp.zeros((rows, stencil.shape[1]), jnp.float32)
    for distance in range(6):
        count = jnp.zeros((rows, stencil.shape[1]), jnp.float32)
        for member in range(6):
            count = count + (slots == stencil[6 * distance + member][None, :]).astype(jnp.float32)
        total = total + WEIGHTS[distance + 1] * count
    return total


def selection_matrix(send_list, live_slots, points):
    slots = lax.broadcasted_iota(jnp.int32, (points, send_list.shape[1]), 0)
    down = (slots == send_list[1][None, :]) & live_slots[1][None, :]
    up = (slots == send_list[0][None, :]) & live_slots[0][None, :]
    return jnp.concatenate([down, up], axis=1).astype(jnp.float32)


def apply_operator(values, potential, pick, near_local, near_below, near_above):
    capacity = pick.shape[1] // 2
    count = lax.axis_size("domain")
    outgoing = dense(values, pick)
    forward = [(i, i + 1) for i in range(count - 1)]
    backward = [(i + 1, i) for i in range(count - 1)]
    from_below = lax.ppermute(outgoing[:, capacity:], "domain", forward)
    from_above = lax.ppermute(outgoing[:, :capacity], "domain", backward)
    near_sum = dense(values, near_local) + dense(from_below, near_below) + dense(from_above, near_above)
    return potential * values - KINETIC * (3.0 * WEIGHTS[0] * values + near_sum)


def filter_block(orbitals, operator_fn, lowest, highest):
    top_bound = highest + SPECTRAL_REACH
    cut_point = lowest + CUT_SHARE * (top_bound - lowest)
    half_width = (top_bound - cut_point) / 2.0
    centre = (top_bound + cut_point) / 2.0
    sigma_now = half_width / (lowest - centre)
    sigma_scale = 2.0 / sigma_now
    previous = orbitals
    current = sigma_now / half_width * (operator_fn(orbitals) - centre * orbitals)
    for order_index in range(2, DEGREE + 1):
        sigma_next = 1.0 / (sigma_scale - sigma_now)
        following = (
            2.0 * sigma_next / half_width * (operator_fn(current) - centre * current)
            - sigma_now * sigma_next * previous
        )
        previous = current
        current = following
        sigma_now = sigma_next
    return current


def inner_products(left_block, right_block):
    return lax.dot_general(
        left_block,
        right_block,
        (((1,), (1,)), ((), ())),
        precision=lax.Precision.HIGHEST,
        preferred_element_type=jnp.float32,
    )


def exchange(value, axis, step):
    count = lax.axis_size(axis)
    return lax.ppermute(value, axis, [(i, i ^ step) for i in range(count)])


def butterfly_max(value, axis):
    step = 1
    while step < lax.axis_size(axis):
        value = jnp.maximum(value, exchange(value, axis, step))
        step *= 2
    return value


def gather_blocks(block, axis, steps):
    index = lax.axis_index(axis)
    gathered = block
    for step in steps:
        received = exchange(gathered, axis, step)
        high = (index & step) != 0
        gathered = jnp.stack(
            [jnp.where(high, received, gathered), jnp.where(high, gathered, received)]
        )
    return gathered


def scatter_sum(parts, axis, steps):
    index = lax.axis_index(axis)
    current = parts
    for position, step in enumerate(steps):
        high = (index & step) != 0
        low_half = lax.index_in_dim(current, 0, axis=position + 1, keepdims=False)
        high_half = lax.index_in_dim(current, 1, axis=position + 1, keepdims=False)
        keep = jnp.where(high, high_half, low_half)
        send = jnp.where(high, low_half, high_half)
        current = keep + exchange(send, axis, step)
        current = jnp.expand_dims(current, position + 1)
    return current


def shards(orbitals, potential, stencil, send_list, send_count):
    rows, points = orbitals.shape
    capacity = send_list.shape[1]
    domain_count = lax.axis_size("domain")
    band_count = lax.axis_size("band")
    total_points = points * domain_count
    extremes = butterfly_max(jnp.stack([-jnp.min(potential), jnp.max(potential)]), "domain")
    lowest = -extremes[0]
    highest = extremes[1]
    live_slots = lax.broadcasted_iota(jnp.int32, (2, capacity), 1) < send_count

    pick = selection_matrix(send_list, live_slots, points)
    weight = stencil_matrix(stencil, points + 2 * capacity)
    near_local = weight[:points]
    near_below = weight[points : points + capacity]
    near_above = weight[points + capacity :]

    def operator_fn(values):
        return apply_operator(values, potential, pick, near_local, near_below, near_above)

    filtered = filter_block(orbitals, operator_fn, lowest, highest)
    applied = operator_fn(filtered)
    both = jnp.stack([filtered, applied])
    band_steps = (8, 4, 1, 2)
    gathered = gather_blocks(both, "band", band_steps)
    parts = jnp.einsum(
        "rq,abcdsjq->srdcabj",
        filtered,
        gathered,
        precision=lax.Precision.HIGHEST,
        preferred_element_type=jnp.float32,
    )
    parts = jnp.transpose(parts, (0, 1, 5, 4, 3, 2, 6)).reshape(2 * rows, 2, 2, 2, 2, rows)
    sums = scatter_sum(parts, "domain", (1, 2, 4, 8)).reshape(2, rows, rows)
    return (filtered, sums[0] / total_points, sums[1] / total_points)


def solution(mesh):
    placed = (
        P("band", "domain"),
        P("domain"),
        P(None, "domain"),
        P(None, "domain"),
        P(None, "domain"),
    )
    return jax.shard_map(
        shards,
        mesh=mesh,
        in_specs=placed,
        out_specs=(P("band", "domain"), P("band", "domain"), P("band", "domain")),
        check_vma=False,
    )
```

```python
import jax
import jax.numpy as jnp
from jax import lax
from jax.sharding import PartitionSpec as P

DEGREE = 4


WEIGHTS = (
    -5369.0 / 1800.0,
    12.0 / 7.0,
    -15.0 / 56.0,
    10.0 / 189.0,
    -1.0 / 112.0,
    2.0 / 1925.0,
    -1.0 / 16632.0,
)
KINETIC = 50.0 / 9.0
CUT_SHARE = 0.1
SPECTRAL_REACH = (
    KINETIC
    * 3.0
    * (
        abs(WEIGHTS[0])
        + 2.0
        * (
            abs(WEIGHTS[1])
            + abs(WEIGHTS[2])
            + abs(WEIGHTS[3])
            + abs(WEIGHTS[4])
            + abs(WEIGHTS[5])
            + abs(WEIGHTS[6])
        )
    )
)


def dense(left, right):
    return lax.dot_general(
        left,
        right,
        (((1,), (0,)), ((), ())),
        precision=lax.Precision.HIGHEST,
        preferred_element_type=jnp.float32,
    )


def stencil_matrix(stencil, rows):
    slots = lax.broadcasted_iota(jnp.int32, (rows, stencil.shape[1]), 0)
    total = jnp.zeros((rows, stencil.shape[1]), jnp.float32)
    for distance in range(6):
        count = jnp.zeros((rows, stencil.shape[1]), jnp.float32)
        for member in range(6):
            count = count + (slots == stencil[6 * distance + member][None, :]).astype(jnp.float32)
        total = total + WEIGHTS[distance + 1] * count
    return total


def selection_matrix(send_list, live_slots, points):
    slots = lax.broadcasted_iota(jnp.int32, (points, send_list.shape[1]), 0)
    down = (slots == send_list[1][None, :]) & live_slots[1][None, :]
    up = (slots == send_list[0][None, :]) & live_slots[0][None, :]
    return jnp.concatenate([down, up], axis=1).astype(jnp.float32)


def apply_operator(values, potential, pick, near_local, near_below, near_above):
    capacity = pick.shape[1] // 2
    count = lax.axis_size("domain")
    outgoing = dense(values, pick)
    forward = [(i, i + 1) for i in range(count - 1)]
    backward = [(i + 1, i) for i in range(count - 1)]
    from_below = lax.ppermute(outgoing[:, capacity:], "domain", forward)
    from_above = lax.ppermute(outgoing[:, :capacity], "domain", backward)
    near_sum = dense(values, near_local) + dense(from_below, near_below) + dense(from_above, near_above)
    return potential * values - KINETIC * (3.0 * WEIGHTS[0] * values + near_sum)


def filter_block(orbitals, operator_fn, lowest, highest):
    top_bound = highest + SPECTRAL_REACH
    cut_point = lowest + CUT_SHARE * (top_bound - lowest)
    half_width = (top_bound - cut_point) / 2.0
    centre = (top_bound + cut_point) / 2.0
    sigma_now = half_width / (lowest - centre)
    sigma_scale = 2.0 / sigma_now
    previous = orbitals
    current = sigma_now / half_width * (operator_fn(orbitals) - centre * orbitals)
    for order_index in range(2, DEGREE + 1):
        sigma_next = 1.0 / (sigma_scale - sigma_now)
        following = (
            2.0 * sigma_next / half_width * (operator_fn(current) - centre * current)
            - sigma_now * sigma_next * previous
        )
        previous = current
        current = following
        sigma_now = sigma_next
    return current


def inner_products(left_block, right_block):
    return lax.dot_general(
        left_block,
        right_block,
        (((1,), (1,)), ((), ())),
        precision=lax.Precision.HIGHEST,
        preferred_element_type=jnp.float32,
    )


def exchange(value, axis, step):
    count = lax.axis_size(axis)
    return lax.ppermute(value, axis, [(i, i ^ step) for i in range(count)])


def butterfly_max(value, axis):
    step = 1
    while step < lax.axis_size(axis):
        value = jnp.maximum(value, exchange(value, axis, step))
        step *= 2
    return value


def gather_blocks(block, axis, steps):
    index = lax.axis_index(axis)
    gathered = block
    for step in steps:
        received = exchange(gathered, axis, step)
        high = (index & step) != 0
        gathered = jnp.stack(
            [jnp.where(high, received, gathered), jnp.where(high, gathered, received)]
        )
    return gathered


def scatter_sum(parts, axis, steps):
    index = lax.axis_index(axis)
    current = parts
    for position, step in enumerate(steps):
        high = (index & step) != 0
        low_half = lax.index_in_dim(current, 0, axis=position + 1, keepdims=False)
        high_half = lax.index_in_dim(current, 1, axis=position + 1, keepdims=False)
        keep = jnp.where(high, high_half, low_half)
        send = jnp.where(high, low_half, high_half)
        current = keep + exchange(send, axis, step)
        current = jnp.expand_dims(current, position + 1)
    return current


def shards(orbitals, potential, stencil, send_list, send_count):
    rows, points = orbitals.shape
    capacity = send_list.shape[1]
    domain_count = lax.axis_size("domain")
    band_count = lax.axis_size("band")
    total_points = points * domain_count
    extremes = butterfly_max(jnp.stack([-jnp.min(potential), jnp.max(potential)]), "domain")
    lowest = -extremes[0]
    highest = extremes[1]
    live_slots = lax.broadcasted_iota(jnp.int32, (2, capacity), 1) < send_count

    pick = selection_matrix(send_list, live_slots, points)
    weight = stencil_matrix(stencil, points + 2 * capacity)
    near_local = weight[:points]
    near_below = weight[points : points + capacity]
    near_above = weight[points + capacity :]

    def operator_fn(values):
        return apply_operator(values, potential, pick, near_local, near_below, near_above)

    filtered = filter_block(orbitals, operator_fn, lowest, highest)
    applied = operator_fn(filtered)
    band_steps = (8, 4, 1, 2)
    gathered = gather_blocks(filtered, "band", band_steps)
    both = jnp.stack([filtered, applied])
    parts = jnp.einsum(
        "srq,abcdjq->srdcabj",
        both,
        gathered,
        precision=lax.Precision.HIGHEST,
        preferred_element_type=jnp.float32,
    )
    parts = jnp.transpose(parts, (0, 1, 5, 4, 3, 2, 6)).reshape(2 * rows, 2, 2, 2, 2, rows)
    sums = scatter_sum(parts, "domain", (1, 2, 4, 8)).reshape(2, rows, rows)
    swap = [(b * domain_count + d, d * domain_count + b) for b in range(band_count) for d in range(domain_count)]
    mirrored = lax.ppermute(sums[1], ("band", "domain"), swap)
    sums = jnp.stack([sums[0], mirrored.T])
    return (filtered, sums[0] / total_points, sums[1] / total_points)


def solution(mesh):
    placed = (
        P("band", "domain"),
        P("domain"),
        P(None, "domain"),
        P(None, "domain"),
        P(None, "domain"),
    )
    return jax.shard_map(
        shards,
        mesh=mesh,
        in_specs=placed,
        out_specs=(P("band", "domain"), P("band", "domain"), P("band", "domain")),
        check_vma=False,
    )
```

```python
import jax
import jax.numpy as jnp
from jax import lax
from jax.sharding import PartitionSpec as P

DEGREE = 4


WEIGHTS = (
    -5369.0 / 1800.0,
    12.0 / 7.0,
    -15.0 / 56.0,
    10.0 / 189.0,
    -1.0 / 112.0,
    2.0 / 1925.0,
    -1.0 / 16632.0,
)
KINETIC = 50.0 / 9.0
CUT_SHARE = 0.1
SPECTRAL_REACH = (
    KINETIC
    * 3.0
    * (
        abs(WEIGHTS[0])
        + 2.0
        * (
            abs(WEIGHTS[1])
            + abs(WEIGHTS[2])
            + abs(WEIGHTS[3])
            + abs(WEIGHTS[4])
            + abs(WEIGHTS[5])
            + abs(WEIGHTS[6])
        )
    )
)


def dense(left, right):
    return lax.dot_general(
        left,
        right,
        (((1,), (0,)), ((), ())),
        precision=lax.Precision.HIGHEST,
        preferred_element_type=jnp.float32,
    )


def stencil_matrix(stencil, rows):
    slots = lax.broadcasted_iota(jnp.int32, (rows, stencil.shape[1]), 0)
    total = jnp.zeros((rows, stencil.shape[1]), jnp.float32)
    for distance in range(6):
        count = jnp.zeros((rows, stencil.shape[1]), jnp.float32)
        for member in range(6):
            count = count + (slots == stencil[6 * distance + member][None, :]).astype(jnp.float32)
        total = total + WEIGHTS[distance + 1] * count
    return total


def selection_matrix(send_list, live_slots, points):
    slots = lax.broadcasted_iota(jnp.int32, (points, send_list.shape[1]), 0)
    down = (slots == send_list[1][None, :]) & live_slots[1][None, :]
    up = (slots == send_list[0][None, :]) & live_slots[0][None, :]
    return jnp.concatenate([down, up], axis=1).astype(jnp.float32)


def apply_operator(values, potential, pick, near_local, near_below, near_above):
    capacity = pick.shape[1] // 2
    count = lax.axis_size("domain")
    outgoing = dense(values, pick)
    forward = [(i, i + 1) for i in range(count - 1)]
    backward = [(i + 1, i) for i in range(count - 1)]
    from_below = lax.ppermute(outgoing[:, capacity:], "domain", forward)
    from_above = lax.ppermute(outgoing[:, :capacity], "domain", backward)
    near_sum = dense(values, near_local) + dense(from_below, near_below) + dense(from_above, near_above)
    return potential * values - KINETIC * (3.0 * WEIGHTS[0] * values + near_sum)


def filter_block(orbitals, operator_fn, lowest, highest):
    top_bound = highest + SPECTRAL_REACH
    cut_point = lowest + CUT_SHARE * (top_bound - lowest)
    half_width = (top_bound - cut_point) / 2.0
    centre = (top_bound + cut_point) / 2.0
    sigma_now = half_width / (lowest - centre)
    sigma_scale = 2.0 / sigma_now
    previous = orbitals
    current = sigma_now / half_width * (operator_fn(orbitals) - centre * orbitals)
    for order_index in range(2, DEGREE + 1):
        sigma_next = 1.0 / (sigma_scale - sigma_now)
        following = (
            2.0 * sigma_next / half_width * (operator_fn(current) - centre * current)
            - sigma_now * sigma_next * previous
        )
        previous = current
        current = following
        sigma_now = sigma_next
    return current


def inner_products(left_block, right_block):
    return lax.dot_general(
        left_block,
        right_block,
        (((1,), (1,)), ((), ())),
        precision=lax.Precision.HIGHEST,
        preferred_element_type=jnp.float32,
    )


def exchange(value, axis, step):
    count = lax.axis_size(axis)
    return lax.ppermute(value, axis, [(i, i ^ step) for i in range(count)])


def butterfly_max(value, axis):
    step = 1
    while step < lax.axis_size(axis):
        value = jnp.maximum(value, exchange(value, axis, step))
        step *= 2
    return value


def gather_blocks(block, axis, steps):
    index = lax.axis_index(axis)
    gathered = block
    for step in steps:
        received = exchange(gathered, axis, step)
        high = (index & step) != 0
        gathered = jnp.stack(
            [jnp.where(high, received, gathered), jnp.where(high, gathered, received)]
        )
    return gathered


def scatter_sum(parts, axis, steps):
    index = lax.axis_index(axis)
    current = parts
    for position, step in enumerate(steps):
        high = (index & step) != 0
        low_half = lax.index_in_dim(current, 0, axis=position + 1, keepdims=False)
        high_half = lax.index_in_dim(current, 1, axis=position + 1, keepdims=False)
        keep = jnp.where(high, high_half, low_half)
        send = jnp.where(high, low_half, high_half)
        current = keep + exchange(send, axis, step)
        current = jnp.expand_dims(current, position + 1)
    return current


def exchange_all(value, axis):
    count = lax.axis_size(axis)
    spread = jnp.broadcast_to(value[None], (count,) + value.shape)
    return lax.all_to_all(spread, axis, 0, 0, tiled=True)


def shards(orbitals, potential, stencil, send_list, send_count):
    rows, points = orbitals.shape
    capacity = send_list.shape[1]
    domain_count = lax.axis_size("domain")
    band_count = lax.axis_size("band")
    total_points = points * domain_count
    local_extremes = jnp.stack([-jnp.min(potential), jnp.max(potential)])
    extremes = jnp.max(exchange_all(local_extremes, "domain"), axis=0)
    lowest = -extremes[0]
    highest = extremes[1]
    live_slots = lax.broadcasted_iota(jnp.int32, (2, capacity), 1) < send_count

    pick = selection_matrix(send_list, live_slots, points)
    weight = stencil_matrix(stencil, points + 2 * capacity)
    near_local = weight[:points]
    near_below = weight[points : points + capacity]
    near_above = weight[points + capacity :]

    def operator_fn(values):
        return apply_operator(values, potential, pick, near_local, near_below, near_above)

    filtered = filter_block(orbitals, operator_fn, lowest, highest)
    applied = operator_fn(filtered)
    gathered = exchange_all(filtered, "band").reshape(band_count * rows, points)
    both = jnp.stack([filtered, applied])
    parts = jnp.einsum(
        "srq,jq->srj",
        both,
        gathered,
        precision=lax.Precision.HIGHEST,
        preferred_element_type=jnp.float32,
    )
    blocks = jnp.transpose(parts.reshape(2, rows, domain_count, rows), (2, 0, 1, 3))
    sums = jnp.sum(lax.all_to_all(blocks, "domain", 0, 0, tiled=True), axis=0)
    swap = [(b * domain_count + d, d * domain_count + b) for b in range(band_count) for d in range(domain_count)]
    mirrored = lax.ppermute(sums[1], ("band", "domain"), swap)
    sums = jnp.stack([sums[0], mirrored.T])
    return (filtered, sums[0] / total_points, sums[1] / total_points)


def solution(mesh):
    placed = (
        P("band", "domain"),
        P("domain"),
        P(None, "domain"),
        P(None, "domain"),
        P(None, "domain"),
    )
    return jax.shard_map(
        shards,
        mesh=mesh,
        in_specs=placed,
        out_specs=(P("band", "domain"), P("band", "domain"), P("band", "domain")),
        check_vma=False,
    )
```

```python
import jax
import jax.numpy as jnp
from jax import lax
from jax.sharding import PartitionSpec as P

DEGREE = 4


WEIGHTS = (
    -5369.0 / 1800.0,
    12.0 / 7.0,
    -15.0 / 56.0,
    10.0 / 189.0,
    -1.0 / 112.0,
    2.0 / 1925.0,
    -1.0 / 16632.0,
)
KINETIC = 50.0 / 9.0
CUT_SHARE = 0.1
SPECTRAL_REACH = (
    KINETIC
    * 3.0
    * (
        abs(WEIGHTS[0])
        + 2.0
        * (
            abs(WEIGHTS[1])
            + abs(WEIGHTS[2])
            + abs(WEIGHTS[3])
            + abs(WEIGHTS[4])
            + abs(WEIGHTS[5])
            + abs(WEIGHTS[6])
        )
    )
)


def dense(left, right):
    return lax.dot_general(
        left,
        right,
        (((1,), (0,)), ((), ())),
        precision=lax.Precision.HIGHEST,
        preferred_element_type=jnp.float32,
    )


def stencil_matrix(stencil, rows):
    slots = lax.broadcasted_iota(jnp.int32, (rows, stencil.shape[1]), 0)
    total = jnp.zeros((rows, stencil.shape[1]), jnp.float32)
    for distance in range(6):
        count = jnp.zeros((rows, stencil.shape[1]), jnp.float32)
        for member in range(6):
            count = count + (slots == stencil[6 * distance + member][None, :]).astype(jnp.float32)
        total = total + WEIGHTS[distance + 1] * count
    return total


def selection_matrix(send_list, live_slots, points):
    slots = lax.broadcasted_iota(jnp.int32, (points, send_list.shape[1]), 0)
    down = (slots == send_list[1][None, :]) & live_slots[1][None, :]
    up = (slots == send_list[0][None, :]) & live_slots[0][None, :]
    return jnp.concatenate([down, up], axis=1).astype(jnp.float32)


def apply_operator(values, potential, pick, near_local, near_below, near_above):
    capacity = pick.shape[1] // 2
    count = lax.axis_size("domain")
    outgoing = dense(values, pick)
    forward = [(i, i + 1) for i in range(count - 1)]
    backward = [(i + 1, i) for i in range(count - 1)]
    from_below = lax.ppermute(outgoing[:, capacity:], "domain", forward)
    from_above = lax.ppermute(outgoing[:, :capacity], "domain", backward)
    near_sum = dense(values, near_local) + dense(from_below, near_below) + dense(from_above, near_above)
    return potential * values - KINETIC * (3.0 * WEIGHTS[0] * values + near_sum)


def filter_block(orbitals, operator_fn, lowest, highest):
    top_bound = highest + SPECTRAL_REACH
    cut_point = lowest + CUT_SHARE * (top_bound - lowest)
    half_width = (top_bound - cut_point) / 2.0
    centre = (top_bound + cut_point) / 2.0
    sigma_now = half_width / (lowest - centre)
    sigma_scale = 2.0 / sigma_now
    previous = orbitals
    current = sigma_now / half_width * (operator_fn(orbitals) - centre * orbitals)
    for order_index in range(2, DEGREE + 1):
        sigma_next = 1.0 / (sigma_scale - sigma_now)
        following = (
            2.0 * sigma_next / half_width * (operator_fn(current) - centre * current)
            - sigma_now * sigma_next * previous
        )
        previous = current
        current = following
        sigma_now = sigma_next
    return current


def inner_products(left_block, right_block):
    return lax.dot_general(
        left_block,
        right_block,
        (((1,), (1,)), ((), ())),
        precision=lax.Precision.HIGHEST,
        preferred_element_type=jnp.float32,
    )


def exchange(value, axis, step):
    count = lax.axis_size(axis)
    return lax.ppermute(value, axis, [(i, i ^ step) for i in range(count)])


def butterfly_max(value, axis):
    step = 1
    while step < lax.axis_size(axis):
        value = jnp.maximum(value, exchange(value, axis, step))
        step *= 2
    return value


def gather_blocks(block, axis, steps):
    index = lax.axis_index(axis)
    gathered = block
    for step in steps:
        received = exchange(gathered, axis, step)
        high = (index & step) != 0
        gathered = jnp.stack(
            [jnp.where(high, received, gathered), jnp.where(high, gathered, received)]
        )
    return gathered


def scatter_sum(parts, axis, steps):
    index = lax.axis_index(axis)
    current = parts
    for position, step in enumerate(steps):
        high = (index & step) != 0
        low_half = lax.index_in_dim(current, 0, axis=position + 1, keepdims=False)
        high_half = lax.index_in_dim(current, 1, axis=position + 1, keepdims=False)
        keep = jnp.where(high, high_half, low_half)
        send = jnp.where(high, low_half, high_half)
        current = keep + exchange(send, axis, step)
        current = jnp.expand_dims(current, position + 1)
    return current


def exchange_all(value, axis):
    count = lax.axis_size(axis)
    spread = jnp.broadcast_to(value[None], (count,) + value.shape)
    return lax.all_to_all(spread, axis, 0, 0, tiled=True)


def shards(orbitals, potential, stencil, send_list, send_count):
    rows, points = orbitals.shape
    capacity = send_list.shape[1]
    domain_count = lax.axis_size("domain")
    band_count = lax.axis_size("band")
    total_points = points * domain_count
    panel = exchange_all(orbitals, "band").reshape(band_count * rows, points)
    local_extremes = jnp.stack([-jnp.min(potential), jnp.max(potential)])
    extremes = jnp.max(exchange_all(local_extremes, "domain"), axis=0)
    lowest = -extremes[0]
    highest = extremes[1]
    live_slots = lax.broadcasted_iota(jnp.int32, (2, capacity), 1) < send_count

    pick = selection_matrix(send_list, live_slots, points)
    weight = stencil_matrix(stencil, points + 2 * capacity)
    near_local = weight[:points]
    near_below = weight[points : points + capacity]
    near_above = weight[points + capacity :]

    def operator_fn(values):
        return apply_operator(values, potential, pick, near_local, near_below, near_above)

    filtered_panel = filter_block(panel, operator_fn, lowest, highest)
    applied_panel = operator_fn(filtered_panel)
    band_index = lax.axis_index("band")
    filtered = lax.dynamic_slice_in_dim(filtered_panel, band_index * rows, rows, axis=0)
    parts = jnp.stack(
        [inner_products(filtered, filtered_panel), inner_products(filtered, applied_panel)]
    )
    blocks = jnp.transpose(parts.reshape(2, rows, domain_count, rows), (2, 0, 1, 3))
    sums = jnp.sum(lax.all_to_all(blocks, "domain", 0, 0, tiled=True), axis=0)
    return (filtered, sums[0] / total_points, sums[1] / total_points)


def solution(mesh):
    placed = (
        P("band", "domain"),
        P("domain"),
        P(None, "domain"),
        P(None, "domain"),
        P(None, "domain"),
    )
    return jax.shard_map(
        shards,
        mesh=mesh,
        in_specs=placed,
        out_specs=(P("band", "domain"), P("band", "domain"), P("band", "domain")),
        check_vma=False,
    )
```

```python
import jax
import jax.numpy as jnp
from jax import lax
from jax.sharding import PartitionSpec as P

DEGREE = 4


WEIGHTS = (
    -5369.0 / 1800.0,
    12.0 / 7.0,
    -15.0 / 56.0,
    10.0 / 189.0,
    -1.0 / 112.0,
    2.0 / 1925.0,
    -1.0 / 16632.0,
)
KINETIC = 50.0 / 9.0
CUT_SHARE = 0.1
SPECTRAL_REACH = (
    KINETIC
    * 3.0
    * (
        abs(WEIGHTS[0])
        + 2.0
        * (
            abs(WEIGHTS[1])
            + abs(WEIGHTS[2])
            + abs(WEIGHTS[3])
            + abs(WEIGHTS[4])
            + abs(WEIGHTS[5])
            + abs(WEIGHTS[6])
        )
    )
)


def dense(left, right):
    return lax.dot_general(
        left,
        right,
        (((1,), (0,)), ((), ())),
        precision=lax.Precision.HIGHEST,
        preferred_element_type=jnp.float32,
    )


def stencil_matrix(stencil, rows):
    slots = lax.broadcasted_iota(jnp.int32, (rows, stencil.shape[1]), 0)
    total = jnp.zeros((rows, stencil.shape[1]), jnp.float32)
    for distance in range(6):
        count = jnp.zeros((rows, stencil.shape[1]), jnp.float32)
        for member in range(6):
            count = count + (slots == stencil[6 * distance + member][None, :]).astype(jnp.float32)
        total = total + WEIGHTS[distance + 1] * count
    return total


def selection_matrix(send_list, live_slots, points):
    slots = lax.broadcasted_iota(jnp.int32, (points, send_list.shape[1]), 0)
    down = (slots == send_list[1][None, :]) & live_slots[1][None, :]
    up = (slots == send_list[0][None, :]) & live_slots[0][None, :]
    return jnp.concatenate([down, up], axis=1).astype(jnp.float32)


def apply_operator(values, potential, pick, near_local, near_below, near_above):
    capacity = pick.shape[1] // 2
    count = lax.axis_size("domain")
    outgoing = dense(values, pick)
    forward = [(i, (i + 1) % count) for i in range(count)]
    backward = [((i + 1) % count, i) for i in range(count)]
    from_below = lax.ppermute(outgoing[:, capacity:], "domain", forward)
    from_above = lax.ppermute(outgoing[:, :capacity], "domain", backward)
    near_sum = dense(values, near_local) + dense(from_below, near_below) + dense(from_above, near_above)
    return potential * values - KINETIC * (3.0 * WEIGHTS[0] * values + near_sum)


def filter_block(orbitals, operator_fn, lowest, highest):
    top_bound = highest + SPECTRAL_REACH
    cut_point = lowest + CUT_SHARE * (top_bound - lowest)
    half_width = (top_bound - cut_point) / 2.0
    centre = (top_bound + cut_point) / 2.0
    sigma_now = half_width / (lowest - centre)
    sigma_scale = 2.0 / sigma_now
    previous = orbitals
    current = sigma_now / half_width * (operator_fn(orbitals) - centre * orbitals)
    for order_index in range(2, DEGREE + 1):
        sigma_next = 1.0 / (sigma_scale - sigma_now)
        following = (
            2.0 * sigma_next / half_width * (operator_fn(current) - centre * current)
            - sigma_now * sigma_next * previous
        )
        previous = current
        current = following
        sigma_now = sigma_next
    return current


def inner_products(left_block, right_block):
    return lax.dot_general(
        left_block,
        right_block,
        (((1,), (1,)), ((), ())),
        precision=lax.Precision.HIGHEST,
        preferred_element_type=jnp.float32,
    )


def exchange(value, axis, step):
    count = lax.axis_size(axis)
    return lax.ppermute(value, axis, [(i, i ^ step) for i in range(count)])


def butterfly_max(value, axis):
    step = 1
    while step < lax.axis_size(axis):
        value = jnp.maximum(value, exchange(value, axis, step))
        step *= 2
    return value


def gather_blocks(block, axis, steps):
    index = lax.axis_index(axis)
    gathered = block
    for step in steps:
        received = exchange(gathered, axis, step)
        high = (index & step) != 0
        gathered = jnp.stack(
            [jnp.where(high, received, gathered), jnp.where(high, gathered, received)]
        )
    return gathered


def scatter_sum(parts, axis, steps):
    index = lax.axis_index(axis)
    current = parts
    for position, step in enumerate(steps):
        high = (index & step) != 0
        low_half = lax.index_in_dim(current, 0, axis=position + 1, keepdims=False)
        high_half = lax.index_in_dim(current, 1, axis=position + 1, keepdims=False)
        keep = jnp.where(high, high_half, low_half)
        send = jnp.where(high, low_half, high_half)
        current = keep + exchange(send, axis, step)
        current = jnp.expand_dims(current, position + 1)
    return current


def exchange_all(value, axis):
    count = lax.axis_size(axis)
    spread = jnp.broadcast_to(value[None], (count,) + value.shape)
    return lax.all_to_all(spread, axis, 0, 0, tiled=True)


def shards(orbitals, potential, stencil, send_list, send_count):
    rows, points = orbitals.shape
    capacity = send_list.shape[1]
    domain_count = lax.axis_size("domain")
    band_count = lax.axis_size("band")
    total_points = points * domain_count
    panel = exchange_all(orbitals, "band").reshape(band_count * rows, points)
    local_extremes = jnp.stack([-jnp.min(potential), jnp.max(potential)])
    extremes = jnp.max(exchange_all(local_extremes, "domain"), axis=0)
    lowest = -extremes[0]
    highest = extremes[1]
    live_slots = lax.broadcasted_iota(jnp.int32, (2, capacity), 1) < send_count

    pick = selection_matrix(send_list, live_slots, points)
    weight = stencil_matrix(stencil, points + 2 * capacity)
    near_local = weight[:points]
    near_below = weight[points : points + capacity]
    near_above = weight[points + capacity :]

    def operator_fn(values):
        return apply_operator(values, potential, pick, near_local, near_below, near_above)

    filtered_panel = filter_block(panel, operator_fn, lowest, highest)
    applied_panel = operator_fn(filtered_panel)
    band_index = lax.axis_index("band")
    filtered = lax.dynamic_slice_in_dim(filtered_panel, band_index * rows, rows, axis=0)
    parts = jnp.stack(
        [inner_products(filtered, filtered_panel), inner_products(filtered, applied_panel)]
    )
    blocks = jnp.transpose(parts.reshape(2, rows, domain_count, rows), (2, 0, 1, 3))
    sums = jnp.sum(lax.all_to_all(blocks, "domain", 0, 0, tiled=True), axis=0)
    return (filtered, sums[0] / total_points, sums[1] / total_points)


def solution(mesh):
    placed = (
        P("band", "domain"),
        P("domain"),
        P(None, "domain"),
        P(None, "domain"),
        P(None, "domain"),
    )
    return jax.shard_map(
        shards,
        mesh=mesh,
        in_specs=placed,
        out_specs=(P("band", "domain"), P("band", "domain"), P("band", "domain")),
        check_vma=False,
    )
```

```python
import jax
import jax.numpy as jnp
from jax import lax
from jax.sharding import PartitionSpec as P

DEGREE = 4


WEIGHTS = (
    -5369.0 / 1800.0,
    12.0 / 7.0,
    -15.0 / 56.0,
    10.0 / 189.0,
    -1.0 / 112.0,
    2.0 / 1925.0,
    -1.0 / 16632.0,
)
KINETIC = 50.0 / 9.0
CUT_SHARE = 0.1
SPECTRAL_REACH = (
    KINETIC
    * 3.0
    * (
        abs(WEIGHTS[0])
        + 2.0
        * (
            abs(WEIGHTS[1])
            + abs(WEIGHTS[2])
            + abs(WEIGHTS[3])
            + abs(WEIGHTS[4])
            + abs(WEIGHTS[5])
            + abs(WEIGHTS[6])
        )
    )
)


def dense(left, right):
    return lax.dot_general(
        left,
        right,
        (((1,), (0,)), ((), ())),
        precision=lax.Precision.HIGHEST,
        preferred_element_type=jnp.float32,
    )


def stencil_matrix(stencil, rows):
    slots = lax.broadcasted_iota(jnp.int32, (rows, stencil.shape[1]), 0)
    total = jnp.zeros((rows, stencil.shape[1]), jnp.float32)
    for distance in range(6):
        count = jnp.zeros((rows, stencil.shape[1]), jnp.float32)
        for member in range(6):
            count = count + (slots == stencil[6 * distance + member][None, :]).astype(jnp.float32)
        total = total + WEIGHTS[distance + 1] * count
    return total


def selection_matrix(send_list, live_slots, points):
    slots = lax.broadcasted_iota(jnp.int32, (points, send_list.shape[1]), 0)
    down = (slots == send_list[1][None, :]) & live_slots[1][None, :]
    up = (slots == send_list[0][None, :]) & live_slots[0][None, :]
    return jnp.concatenate([down, up], axis=1).astype(jnp.float32)


def apply_operator(values, potential, pick, near_local, near_below, near_above):
    capacity = pick.shape[1] // 2
    count = lax.axis_size("domain")
    outgoing = dense(values, pick)
    forward = [(i, (i + 1) % count) for i in range(count)]
    backward = [((i + 1) % count, i) for i in range(count)]
    from_below = lax.ppermute(outgoing[:, capacity:], "domain", forward)
    from_above = lax.ppermute(outgoing[:, :capacity], "domain", backward)
    near_sum = dense(values, near_local) + dense(from_below, near_below) + dense(from_above, near_above)
    return potential * values - KINETIC * (3.0 * WEIGHTS[0] * values + near_sum)


def filter_block(orbitals, operator_fn, lowest, highest):
    top_bound = highest + SPECTRAL_REACH
    cut_point = lowest + CUT_SHARE * (top_bound - lowest)
    half_width = (top_bound - cut_point) / 2.0
    centre = (top_bound + cut_point) / 2.0
    sigma_now = half_width / (lowest - centre)
    sigma_scale = 2.0 / sigma_now
    previous = orbitals
    current = sigma_now / half_width * (operator_fn(orbitals) - centre * orbitals)
    for order_index in range(2, DEGREE + 1):
        sigma_next = 1.0 / (sigma_scale - sigma_now)
        following = (
            2.0 * sigma_next / half_width * (operator_fn(current) - centre * current)
            - sigma_now * sigma_next * previous
        )
        previous = current
        current = following
        sigma_now = sigma_next
    return current


def inner_products(left_block, right_block):
    return lax.dot_general(
        left_block,
        right_block,
        (((1,), (1,)), ((), ())),
        precision=lax.Precision.HIGHEST,
        preferred_element_type=jnp.float32,
    )


def exchange(value, axis, step):
    count = lax.axis_size(axis)
    return lax.ppermute(value, axis, [(i, i ^ step) for i in range(count)])


def butterfly_max(value, axis):
    step = 1
    while step < lax.axis_size(axis):
        value = jnp.maximum(value, exchange(value, axis, step))
        step *= 2
    return value


def gather_blocks(block, axis, steps):
    index = lax.axis_index(axis)
    gathered = block
    for step in steps:
        received = exchange(gathered, axis, step)
        high = (index & step) != 0
        gathered = jnp.stack(
            [jnp.where(high, received, gathered), jnp.where(high, gathered, received)]
        )
    return gathered


def scatter_sum(parts, axis, steps):
    index = lax.axis_index(axis)
    current = parts
    for position, step in enumerate(steps):
        high = (index & step) != 0
        low_half = lax.index_in_dim(current, 0, axis=position + 1, keepdims=False)
        high_half = lax.index_in_dim(current, 1, axis=position + 1, keepdims=False)
        keep = jnp.where(high, high_half, low_half)
        send = jnp.where(high, low_half, high_half)
        current = keep + exchange(send, axis, step)
        current = jnp.expand_dims(current, position + 1)
    return current


def exchange_all(value, axis):
    count = lax.axis_size(axis)
    spread = jnp.broadcast_to(value[None], (count,) + value.shape)
    return lax.all_to_all(spread, axis, 0, 0, tiled=True)


def rotated(value, axis):
    count = lax.axis_size(axis)
    received = [value]
    for shift in range(1, count):
        pairs = [((i + shift) % count, i) for i in range(count)]
        received.append(lax.ppermute(value, axis, pairs))
    return jnp.stack(received)


def shards(orbitals, potential, stencil, send_list, send_count):
    rows, points = orbitals.shape
    capacity = send_list.shape[1]
    domain_count = lax.axis_size("domain")
    band_count = lax.axis_size("band")
    total_points = points * domain_count
    panel = rotated(orbitals, "band").reshape(band_count * rows, points)
    local_extremes = jnp.stack([-jnp.min(potential), jnp.max(potential)])
    extremes = jnp.max(rotated(local_extremes, "domain"), axis=0)
    lowest = -extremes[0]
    highest = extremes[1]
    live_slots = lax.broadcasted_iota(jnp.int32, (2, capacity), 1) < send_count

    pick = selection_matrix(send_list, live_slots, points)
    weight = stencil_matrix(stencil, points + 2 * capacity)
    near_local = weight[:points]
    near_below = weight[points : points + capacity]
    near_above = weight[points + capacity :]

    def operator_fn(values):
        return apply_operator(values, potential, pick, near_local, near_below, near_above)

    filtered_panel = filter_block(panel, operator_fn, lowest, highest)
    applied_panel = operator_fn(filtered_panel)
    band_index = lax.axis_index("band")
    filtered = filtered_panel[:rows]
    parts = jnp.stack(
        [inner_products(filtered, filtered_panel), inner_products(filtered, applied_panel)]
    )
    parts = jnp.roll(parts.reshape(2, rows, band_count, rows), band_index, axis=2)
    blocks = jnp.transpose(parts, (2, 0, 1, 3))
    sums = jnp.sum(lax.all_to_all(blocks, "domain", 0, 0, tiled=True), axis=0)
    return (filtered, sums[0] / total_points, sums[1] / total_points)


def solution(mesh):
    placed = (
        P("band", "domain"),
        P("domain"),
        P(None, "domain"),
        P(None, "domain"),
        P(None, "domain"),
    )
    return jax.shard_map(
        shards,
        mesh=mesh,
        in_specs=placed,
        out_specs=(P("band", "domain"), P("band", "domain"), P("band", "domain")),
        check_vma=False,
    )
```

```python
import jax
import jax.numpy as jnp
from jax import lax
from jax.sharding import PartitionSpec as P

DEGREE = 4


WEIGHTS = (
    -5369.0 / 1800.0,
    12.0 / 7.0,
    -15.0 / 56.0,
    10.0 / 189.0,
    -1.0 / 112.0,
    2.0 / 1925.0,
    -1.0 / 16632.0,
)
KINETIC = 50.0 / 9.0
CUT_SHARE = 0.1
SPECTRAL_REACH = (
    KINETIC
    * 3.0
    * (
        abs(WEIGHTS[0])
        + 2.0
        * (
            abs(WEIGHTS[1])
            + abs(WEIGHTS[2])
            + abs(WEIGHTS[3])
            + abs(WEIGHTS[4])
            + abs(WEIGHTS[5])
            + abs(WEIGHTS[6])
        )
    )
)


def dense(left, right):
    return lax.dot_general(
        left,
        right,
        (((1,), (0,)), ((), ())),
        precision=lax.Precision.HIGHEST,
        preferred_element_type=jnp.float32,
    )


def stencil_matrix(stencil, rows):
    slots = lax.broadcasted_iota(jnp.int32, (rows, stencil.shape[1]), 0)
    total = jnp.zeros((rows, stencil.shape[1]), jnp.float32)
    for distance in range(6):
        count = jnp.zeros((rows, stencil.shape[1]), jnp.float32)
        for member in range(6):
            count = count + (slots == stencil[6 * distance + member][None, :]).astype(jnp.float32)
        total = total + WEIGHTS[distance + 1] * count
    return total


def selection_matrix(send_list, live_slots, points):
    slots = lax.broadcasted_iota(jnp.int32, (points, send_list.shape[1]), 0)
    down = (slots == send_list[1][None, :]) & live_slots[1][None, :]
    up = (slots == send_list[0][None, :]) & live_slots[0][None, :]
    return jnp.concatenate([down, up], axis=1).astype(jnp.float32)


def apply_operator(values, potential, pick, near_local, near_below, near_above):
    capacity = pick.shape[1] // 2
    count = lax.axis_size("domain")
    outgoing = dense(values, pick)
    forward = [(i, (i + 1) % count) for i in range(count)]
    backward = [((i + 1) % count, i) for i in range(count)]
    half = values.shape[0] // 2
    from_below = jnp.concatenate(
        [
            lax.ppermute(outgoing[:half, capacity:], "domain", forward),
            lax.ppermute(outgoing[half:, capacity:], "domain", forward),
        ]
    )
    from_above = jnp.concatenate(
        [
            lax.ppermute(outgoing[:half, :capacity], "domain", backward),
            lax.ppermute(outgoing[half:, :capacity], "domain", backward),
        ]
    )
    near_sum = dense(values, near_local) + dense(from_below, near_below) + dense(from_above, near_above)
    return potential * values - KINETIC * (3.0 * WEIGHTS[0] * values + near_sum)


def filter_block(orbitals, operator_fn, lowest, highest):
    top_bound = highest + SPECTRAL_REACH
    cut_point = lowest + CUT_SHARE * (top_bound - lowest)
    half_width = (top_bound - cut_point) / 2.0
    centre = (top_bound + cut_point) / 2.0
    sigma_now = half_width / (lowest - centre)
    sigma_scale = 2.0 / sigma_now
    previous = orbitals
    current = sigma_now / half_width * (operator_fn(orbitals) - centre * orbitals)
    for order_index in range(2, DEGREE + 1):
        sigma_next = 1.0 / (sigma_scale - sigma_now)
        following = (
            2.0 * sigma_next / half_width * (operator_fn(current) - centre * current)
            - sigma_now * sigma_next * previous
        )
        previous = current
        current = following
        sigma_now = sigma_next
    return current


def inner_products(left_block, right_block):
    return lax.dot_general(
        left_block,
        right_block,
        (((1,), (1,)), ((), ())),
        precision=lax.Precision.HIGHEST,
        preferred_element_type=jnp.float32,
    )


def exchange(value, axis, step):
    count = lax.axis_size(axis)
    return lax.ppermute(value, axis, [(i, i ^ step) for i in range(count)])


def butterfly_max(value, axis):
    step = 1
    while step < lax.axis_size(axis):
        value = jnp.maximum(value, exchange(value, axis, step))
        step *= 2
    return value


def gather_blocks(block, axis, steps):
    index = lax.axis_index(axis)
    gathered = block
    for step in steps:
        received = exchange(gathered, axis, step)
        high = (index & step) != 0
        gathered = jnp.stack(
            [jnp.where(high, received, gathered), jnp.where(high, gathered, received)]
        )
    return gathered


def scatter_sum(parts, axis, steps):
    index = lax.axis_index(axis)
    current = parts
    for position, step in enumerate(steps):
        high = (index & step) != 0
        low_half = lax.index_in_dim(current, 0, axis=position + 1, keepdims=False)
        high_half = lax.index_in_dim(current, 1, axis=position + 1, keepdims=False)
        keep = jnp.where(high, high_half, low_half)
        send = jnp.where(high, low_half, high_half)
        current = keep + exchange(send, axis, step)
        current = jnp.expand_dims(current, position + 1)
    return current


def exchange_all(value, axis):
    count = lax.axis_size(axis)
    spread = jnp.broadcast_to(value[None], (count,) + value.shape)
    return lax.all_to_all(spread, axis, 0, 0, tiled=True)


def shards(orbitals, potential, stencil, send_list, send_count):
    rows, points = orbitals.shape
    capacity = send_list.shape[1]
    domain_count = lax.axis_size("domain")
    band_count = lax.axis_size("band")
    total_points = points * domain_count
    panel = exchange_all(orbitals, "band").reshape(band_count * rows, points)
    local_extremes = jnp.stack([-jnp.min(potential), jnp.max(potential)])
    extremes = jnp.max(exchange_all(local_extremes, "domain"), axis=0)
    lowest = -extremes[0]
    highest = extremes[1]
    live_slots = lax.broadcasted_iota(jnp.int32, (2, capacity), 1) < send_count

    pick = selection_matrix(send_list, live_slots, points)
    weight = stencil_matrix(stencil, points + 2 * capacity)
    near_local = weight[:points]
    near_below = weight[points : points + capacity]
    near_above = weight[points + capacity :]

    def operator_fn(values):
        return apply_operator(values, potential, pick, near_local, near_below, near_above)

    filtered_panel = filter_block(panel, operator_fn, lowest, highest)
    applied_panel = operator_fn(filtered_panel)
    band_index = lax.axis_index("band")
    filtered = lax.dynamic_slice_in_dim(filtered_panel, band_index * rows, rows, axis=0)
    parts = jnp.stack(
        [inner_products(filtered, filtered_panel), inner_products(filtered, applied_panel)]
    )
    blocks = jnp.transpose(parts.reshape(2, rows, domain_count, rows), (2, 0, 1, 3))
    sums = jnp.sum(lax.all_to_all(blocks, "domain", 0, 0, tiled=True), axis=0)
    return (filtered, sums[0] / total_points, sums[1] / total_points)


def solution(mesh):
    placed = (
        P("band", "domain"),
        P("domain"),
        P(None, "domain"),
        P(None, "domain"),
        P(None, "domain"),
    )
    return jax.shard_map(
        shards,
        mesh=mesh,
        in_specs=placed,
        out_specs=(P("band", "domain"), P("band", "domain"), P("band", "domain")),
        check_vma=False,
    )
```

```python
import jax
import jax.numpy as jnp
from jax import lax
from jax.sharding import PartitionSpec as P

DEGREE = 4


WEIGHTS = (
    -5369.0 / 1800.0,
    12.0 / 7.0,
    -15.0 / 56.0,
    10.0 / 189.0,
    -1.0 / 112.0,
    2.0 / 1925.0,
    -1.0 / 16632.0,
)
KINETIC = 50.0 / 9.0
CUT_SHARE = 0.1
SPECTRAL_REACH = (
    KINETIC
    * 3.0
    * (
        abs(WEIGHTS[0])
        + 2.0
        * (
            abs(WEIGHTS[1])
            + abs(WEIGHTS[2])
            + abs(WEIGHTS[3])
            + abs(WEIGHTS[4])
            + abs(WEIGHTS[5])
            + abs(WEIGHTS[6])
        )
    )
)


def dense(left, right):
    return lax.dot_general(
        left,
        right,
        (((1,), (0,)), ((), ())),
        precision=lax.Precision.HIGHEST,
        preferred_element_type=jnp.float32,
    )


def stencil_matrix(stencil, rows):
    slots = lax.broadcasted_iota(jnp.int32, (rows, stencil.shape[1]), 0)
    total = jnp.zeros((rows, stencil.shape[1]), jnp.float32)
    for distance in range(6):
        count = jnp.zeros((rows, stencil.shape[1]), jnp.float32)
        for member in range(6):
            count = count + (slots == stencil[6 * distance + member][None, :]).astype(jnp.float32)
        total = total + WEIGHTS[distance + 1] * count
    return total


def selection_matrix(send_list, live_slots, points):
    slots = lax.broadcasted_iota(jnp.int32, (points, send_list.shape[1]), 0)
    down = (slots == send_list[1][None, :]) & live_slots[1][None, :]
    up = (slots == send_list[0][None, :]) & live_slots[0][None, :]
    return jnp.concatenate([down, up], axis=1).astype(jnp.float32)


def apply_operator(values, potential, pick, near_local, near_below, near_above):
    capacity = pick.shape[1] // 2
    count = lax.axis_size("domain")
    outgoing = dense(values, pick)
    forward = [(i, (i + 1) % count) for i in range(count)]
    backward = [((i + 1) % count, i) for i in range(count)]
    from_below = lax.ppermute(outgoing[:, capacity:], "domain", forward)
    from_above = lax.ppermute(outgoing[:, :capacity], "domain", backward)
    near_sum = dense(values, near_local) + dense(from_above, near_above) + dense(from_below, near_below)
    return potential * values - KINETIC * (3.0 * WEIGHTS[0] * values + near_sum)


def filter_block(orbitals, operator_fn, lowest, highest):
    top_bound = highest + SPECTRAL_REACH
    cut_point = lowest + CUT_SHARE * (top_bound - lowest)
    half_width = (top_bound - cut_point) / 2.0
    centre = (top_bound + cut_point) / 2.0
    sigma_now = half_width / (lowest - centre)
    sigma_scale = 2.0 / sigma_now
    previous = orbitals
    current = sigma_now / half_width * (operator_fn(orbitals) - centre * orbitals)
    for order_index in range(2, DEGREE + 1):
        sigma_next = 1.0 / (sigma_scale - sigma_now)
        following = (
            2.0 * sigma_next / half_width * (operator_fn(current) - centre * current)
            - sigma_now * sigma_next * previous
        )
        previous = current
        current = following
        sigma_now = sigma_next
    return current


def inner_products(left_block, right_block):
    return lax.dot_general(
        left_block,
        right_block,
        (((1,), (1,)), ((), ())),
        precision=lax.Precision.HIGHEST,
        preferred_element_type=jnp.float32,
    )


def exchange(value, axis, step):
    count = lax.axis_size(axis)
    return lax.ppermute(value, axis, [(i, i ^ step) for i in range(count)])


def butterfly_max(value, axis):
    step = 1
    while step < lax.axis_size(axis):
        value = jnp.maximum(value, exchange(value, axis, step))
        step *= 2
    return value


def gather_blocks(block, axis, steps):
    index = lax.axis_index(axis)
    gathered = block
    for step in steps:
        received = exchange(gathered, axis, step)
        high = (index & step) != 0
        gathered = jnp.stack(
            [jnp.where(high, received, gathered), jnp.where(high, gathered, received)]
        )
    return gathered


def scatter_sum(parts, axis, steps):
    index = lax.axis_index(axis)
    current = parts
    for position, step in enumerate(steps):
        high = (index & step) != 0
        low_half = lax.index_in_dim(current, 0, axis=position + 1, keepdims=False)
        high_half = lax.index_in_dim(current, 1, axis=position + 1, keepdims=False)
        keep = jnp.where(high, high_half, low_half)
        send = jnp.where(high, low_half, high_half)
        current = keep + exchange(send, axis, step)
        current = jnp.expand_dims(current, position + 1)
    return current


def exchange_all(value, axis):
    count = lax.axis_size(axis)
    spread = jnp.broadcast_to(value[None], (count,) + value.shape)
    return lax.all_to_all(spread, axis, 0, 0, tiled=True)


def shards(orbitals, potential, stencil, send_list, send_count):
    rows, points = orbitals.shape
    capacity = send_list.shape[1]
    domain_count = lax.axis_size("domain")
    band_count = lax.axis_size("band")
    total_points = points * domain_count
    panel = exchange_all(orbitals, "band").reshape(band_count * rows, points)
    local_extremes = jnp.stack([-jnp.min(potential), jnp.max(potential)])
    extremes = jnp.max(exchange_all(local_extremes, "domain"), axis=0)
    lowest = -extremes[0]
    highest = extremes[1]
    live_slots = lax.broadcasted_iota(jnp.int32, (2, capacity), 1) < send_count

    pick = selection_matrix(send_list, live_slots, points)
    weight = stencil_matrix(stencil, points + 2 * capacity)
    near_local = weight[:points]
    near_below = weight[points : points + capacity]
    near_above = weight[points + capacity :]

    def operator_fn(values):
        return apply_operator(values, potential, pick, near_local, near_below, near_above)

    filtered_panel = filter_block(panel, operator_fn, lowest, highest)
    applied_panel = operator_fn(filtered_panel)
    band_index = lax.axis_index("band")
    filtered = lax.dynamic_slice_in_dim(filtered_panel, band_index * rows, rows, axis=0)
    parts = jnp.stack(
        [inner_products(filtered, filtered_panel), inner_products(filtered, applied_panel)]
    )
    blocks = jnp.transpose(parts.reshape(2, rows, domain_count, rows), (2, 0, 1, 3))
    sums = jnp.sum(lax.all_to_all(blocks, "domain", 0, 0, tiled=True), axis=0)
    return (filtered, sums[0] / total_points, sums[1] / total_points)


def solution(mesh):
    placed = (
        P("band", "domain"),
        P("domain"),
        P(None, "domain"),
        P(None, "domain"),
        P(None, "domain"),
    )
    return jax.shard_map(
        shards,
        mesh=mesh,
        in_specs=placed,
        out_specs=(P("band", "domain"), P("band", "domain"), P("band", "domain")),
        check_vma=False,
    )
```

```python
import jax
import jax.numpy as jnp
from jax import lax
from jax.sharding import PartitionSpec as P

DEGREE = 4


WEIGHTS = (
    -5369.0 / 1800.0,
    12.0 / 7.0,
    -15.0 / 56.0,
    10.0 / 189.0,
    -1.0 / 112.0,
    2.0 / 1925.0,
    -1.0 / 16632.0,
)
KINETIC = 50.0 / 9.0
CUT_SHARE = 0.1
SPECTRAL_REACH = (
    KINETIC
    * 3.0
    * (
        abs(WEIGHTS[0])
        + 2.0
        * (
            abs(WEIGHTS[1])
            + abs(WEIGHTS[2])
            + abs(WEIGHTS[3])
            + abs(WEIGHTS[4])
            + abs(WEIGHTS[5])
            + abs(WEIGHTS[6])
        )
    )
)


def dense(left, right):
    return lax.dot_general(
        left,
        right,
        (((1,), (0,)), ((), ())),
        precision=lax.Precision.HIGHEST,
        preferred_element_type=jnp.float32,
    )


def stencil_matrix(stencil, rows):
    slots = lax.broadcasted_iota(jnp.int32, (rows, stencil.shape[1]), 0)
    total = jnp.zeros((rows, stencil.shape[1]), jnp.float32)
    for distance in range(6):
        count = jnp.zeros((rows, stencil.shape[1]), jnp.float32)
        for member in range(6):
            count = count + (slots == stencil[6 * distance + member][None, :]).astype(jnp.float32)
        total = total + WEIGHTS[distance + 1] * count
    return total


def selection_matrix(send_list, live_slots, points):
    slots = lax.broadcasted_iota(jnp.int32, (points, send_list.shape[1]), 0)
    down = (slots == send_list[1][None, :]) & live_slots[1][None, :]
    up = (slots == send_list[0][None, :]) & live_slots[0][None, :]
    return jnp.concatenate([down, up], axis=1).astype(jnp.float32)


def apply_operator(values, potential, pick, near_local, near_below, near_above):
    capacity = pick.shape[1] // 2
    count = lax.axis_size("domain")
    outgoing = dense(values, pick)
    forward = [(i, (i + 1) % count) for i in range(count)]
    backward = [((i + 1) % count, i) for i in range(count)]
    from_below = lax.ppermute(outgoing[:, capacity:], "domain", forward)
    from_above = lax.ppermute(outgoing[:, :capacity], "domain", backward)
    near_sum = dense(values, near_local) + dense(from_above, near_above) + dense(from_below, near_below)
    return potential * values - KINETIC * (3.0 * WEIGHTS[0] * values + near_sum)


def filter_block(orbitals, operator_fn, lowest, highest):
    top_bound = highest + SPECTRAL_REACH
    cut_point = lowest + CUT_SHARE * (top_bound - lowest)
    half_width = (top_bound - cut_point) / 2.0
    centre = (top_bound + cut_point) / 2.0
    sigma_now = half_width / (lowest - centre)
    sigma_scale = 2.0 / sigma_now
    previous = orbitals
    current = sigma_now / half_width * (operator_fn(orbitals) - centre * orbitals)

    def step(order_index, carried):
        previous, current, sigma_now = carried
        sigma_next = 1.0 / (sigma_scale - sigma_now)
        following = (
            2.0 * sigma_next / half_width * (operator_fn(current) - centre * current)
            - sigma_now * sigma_next * previous
        )
        return current, following, sigma_next

    previous, current, sigma_now = lax.fori_loop(2, DEGREE + 1, step, (previous, current, sigma_now))
    return current


def inner_products(left_block, right_block):
    return lax.dot_general(
        left_block,
        right_block,
        (((1,), (1,)), ((), ())),
        precision=lax.Precision.HIGHEST,
        preferred_element_type=jnp.float32,
    )


def exchange(value, axis, step):
    count = lax.axis_size(axis)
    return lax.ppermute(value, axis, [(i, i ^ step) for i in range(count)])


def butterfly_max(value, axis):
    step = 1
    while step < lax.axis_size(axis):
        value = jnp.maximum(value, exchange(value, axis, step))
        step *= 2
    return value


def gather_blocks(block, axis, steps):
    index = lax.axis_index(axis)
    gathered = block
    for step in steps:
        received = exchange(gathered, axis, step)
        high = (index & step) != 0
        gathered = jnp.stack(
            [jnp.where(high, received, gathered), jnp.where(high, gathered, received)]
        )
    return gathered


def scatter_sum(parts, axis, steps):
    index = lax.axis_index(axis)
    current = parts
    for position, step in enumerate(steps):
        high = (index & step) != 0
        low_half = lax.index_in_dim(current, 0, axis=position + 1, keepdims=False)
        high_half = lax.index_in_dim(current, 1, axis=position + 1, keepdims=False)
        keep = jnp.where(high, high_half, low_half)
        send = jnp.where(high, low_half, high_half)
        current = keep + exchange(send, axis, step)
        current = jnp.expand_dims(current, position + 1)
    return current


def exchange_all(value, axis):
    count = lax.axis_size(axis)
    spread = jnp.broadcast_to(value[None], (count,) + value.shape)
    return lax.all_to_all(spread, axis, 0, 0, tiled=True)


def shards(orbitals, potential, stencil, send_list, send_count):
    rows, points = orbitals.shape
    capacity = send_list.shape[1]
    domain_count = lax.axis_size("domain")
    band_count = lax.axis_size("band")
    total_points = points * domain_count
    panel = exchange_all(orbitals, "band").reshape(band_count * rows, points)
    local_extremes = jnp.stack([-jnp.min(potential), jnp.max(potential)])
    extremes = jnp.max(exchange_all(local_extremes, "domain"), axis=0)
    lowest = -extremes[0]
    highest = extremes[1]
    live_slots = lax.broadcasted_iota(jnp.int32, (2, capacity), 1) < send_count

    pick = selection_matrix(send_list, live_slots, points)
    weight = stencil_matrix(stencil, points + 2 * capacity)
    near_local = weight[:points]
    near_below = weight[points : points + capacity]
    near_above = weight[points + capacity :]

    def operator_fn(values):
        return apply_operator(values, potential, pick, near_local, near_below, near_above)

    filtered_panel = filter_block(panel, operator_fn, lowest, highest)
    applied_panel = operator_fn(filtered_panel)
    band_index = lax.axis_index("band")
    filtered = lax.dynamic_slice_in_dim(filtered_panel, band_index * rows, rows, axis=0)
    parts = jnp.stack(
        [inner_products(filtered, filtered_panel), inner_products(filtered, applied_panel)]
    )
    blocks = jnp.transpose(parts.reshape(2, rows, domain_count, rows), (2, 0, 1, 3))
    sums = jnp.sum(lax.all_to_all(blocks, "domain", 0, 0, tiled=True), axis=0)
    return (filtered, sums[0] / total_points, sums[1] / total_points)


def solution(mesh):
    placed = (
        P("band", "domain"),
        P("domain"),
        P(None, "domain"),
        P(None, "domain"),
        P(None, "domain"),
    )
    return jax.shard_map(
        shards,
        mesh=mesh,
        in_specs=placed,
        out_specs=(P("band", "domain"), P("band", "domain"), P("band", "domain")),
        check_vma=False,
    )
```

```python
import jax
import jax.numpy as jnp
from jax import lax
from jax.sharding import PartitionSpec as P

DEGREE = 4


WEIGHTS = (
    -5369.0 / 1800.0,
    12.0 / 7.0,
    -15.0 / 56.0,
    10.0 / 189.0,
    -1.0 / 112.0,
    2.0 / 1925.0,
    -1.0 / 16632.0,
)
KINETIC = 50.0 / 9.0
CUT_SHARE = 0.1
SPECTRAL_REACH = (
    KINETIC
    * 3.0
    * (
        abs(WEIGHTS[0])
        + 2.0
        * (
            abs(WEIGHTS[1])
            + abs(WEIGHTS[2])
            + abs(WEIGHTS[3])
            + abs(WEIGHTS[4])
            + abs(WEIGHTS[5])
            + abs(WEIGHTS[6])
        )
    )
)


def dense(left, right):
    return lax.dot_general(
        left,
        right,
        (((1,), (0,)), ((), ())),
        precision=lax.Precision.HIGHEST,
        preferred_element_type=jnp.float32,
    )


def stencil_matrix(stencil, rows):
    slots = lax.broadcasted_iota(jnp.int32, (rows, stencil.shape[1]), 0)
    total = jnp.zeros((rows, stencil.shape[1]), jnp.float32)
    for distance in range(6):
        count = jnp.zeros((rows, stencil.shape[1]), jnp.float32)
        for member in range(6):
            count = count + (slots == stencil[6 * distance + member][None, :]).astype(jnp.float32)
        total = total + WEIGHTS[distance + 1] * count
    return total


def selection_matrix(send_list, live_slots, points):
    slots = lax.broadcasted_iota(jnp.int32, (points, send_list.shape[1]), 0)
    down = (slots == send_list[1][None, :]) & live_slots[1][None, :]
    up = (slots == send_list[0][None, :]) & live_slots[0][None, :]
    return jnp.concatenate([down, up], axis=1).astype(jnp.float32)


def apply_operator(values, potential, pick, near_local, near_below, near_above):
    capacity = pick.shape[1] // 2
    count = lax.axis_size("domain")
    outgoing = dense(values, pick)
    forward = [(i, (i + 1) % count) for i in range(count)]
    backward = [((i + 1) % count, i) for i in range(count)]
    from_below = lax.ppermute(outgoing[:, capacity:], "domain", forward)
    from_above = lax.ppermute(outgoing[:, :capacity], "domain", backward)
    near_sum = dense(values, near_local) + dense(from_above, near_above) + dense(from_below, near_below)
    return potential * values - KINETIC * (3.0 * WEIGHTS[0] * values + near_sum)


def filter_block(orbitals, operator_fn, lowest, highest):
    top_bound = highest + SPECTRAL_REACH
    cut_point = lowest + CUT_SHARE * (top_bound - lowest)
    half_width = (top_bound - cut_point) / 2.0
    centre = (top_bound + cut_point) / 2.0
    sigma_now = half_width / (lowest - centre)
    sigma_scale = 2.0 / sigma_now
    previous = orbitals
    current = sigma_now / half_width * (operator_fn(orbitals) - centre * orbitals)
    for order_index in range(2, DEGREE + 1):
        sigma_next = 1.0 / (sigma_scale - sigma_now)
        following = (
            2.0 * sigma_next / half_width * (operator_fn(current) - centre * current)
            - sigma_now * sigma_next * previous
        )
        previous = current
        current = following
        sigma_now = sigma_next
    return current


def inner_products(left_block, right_block):
    return lax.dot_general(
        left_block,
        right_block,
        (((1,), (1,)), ((), ())),
        precision=lax.Precision.HIGHEST,
        preferred_element_type=jnp.float32,
    )


def exchange(value, axis, step):
    count = lax.axis_size(axis)
    return lax.ppermute(value, axis, [(i, i ^ step) for i in range(count)])


def butterfly_max(value, axis):
    step = 1
    while step < lax.axis_size(axis):
        value = jnp.maximum(value, exchange(value, axis, step))
        step *= 2
    return value


def gather_blocks(block, axis, steps):
    index = lax.axis_index(axis)
    gathered = block
    for step in steps:
        received = exchange(gathered, axis, step)
        high = (index & step) != 0
        gathered = jnp.stack(
            [jnp.where(high, received, gathered), jnp.where(high, gathered, received)]
        )
    return gathered


def scatter_sum(parts, axis, steps):
    index = lax.axis_index(axis)
    current = parts
    for position, step in enumerate(steps):
        high = (index & step) != 0
        low_half = lax.index_in_dim(current, 0, axis=position + 1, keepdims=False)
        high_half = lax.index_in_dim(current, 1, axis=position + 1, keepdims=False)
        keep = jnp.where(high, high_half, low_half)
        send = jnp.where(high, low_half, high_half)
        current = keep + exchange(send, axis, step)
        current = jnp.expand_dims(current, position + 1)
    return current


def exchange_all(value, axis):
    count = lax.axis_size(axis)
    spread = jnp.broadcast_to(value[None], (count,) + value.shape)
    return lax.all_to_all(spread, axis, 0, 0, tiled=True)


def shards(orbitals, potential, stencil, send_list, send_count):
    rows, points = orbitals.shape
    capacity = send_list.shape[1]
    domain_count = lax.axis_size("domain")
    band_count = lax.axis_size("band")
    total_points = points * domain_count
    panel = exchange_all(orbitals, "band").reshape(band_count * rows, points)
    local_extremes = jnp.stack([-jnp.min(potential), jnp.max(potential)])
    panel, local_extremes = lax.optimization_barrier((panel, local_extremes))
    extremes = jnp.max(exchange_all(local_extremes, "domain"), axis=0)
    lowest = -extremes[0]
    highest = extremes[1]
    live_slots = lax.broadcasted_iota(jnp.int32, (2, capacity), 1) < send_count

    pick = selection_matrix(send_list, live_slots, points)
    weight = stencil_matrix(stencil, points + 2 * capacity)
    near_local = weight[:points]
    near_below = weight[points : points + capacity]
    near_above = weight[points + capacity :]

    def operator_fn(values):
        return apply_operator(values, potential, pick, near_local, near_below, near_above)

    filtered_panel = filter_block(panel, operator_fn, lowest, highest)
    applied_panel = operator_fn(filtered_panel)
    band_index = lax.axis_index("band")
    filtered = lax.dynamic_slice_in_dim(filtered_panel, band_index * rows, rows, axis=0)
    parts = jnp.stack(
        [inner_products(filtered, filtered_panel), inner_products(filtered, applied_panel)]
    )
    blocks = jnp.transpose(parts.reshape(2, rows, domain_count, rows), (2, 0, 1, 3))
    sums = jnp.sum(lax.all_to_all(blocks, "domain", 0, 0, tiled=True), axis=0)
    return (filtered, sums[0] / total_points, sums[1] / total_points)


def solution(mesh):
    placed = (
        P("band", "domain"),
        P("domain"),
        P(None, "domain"),
        P(None, "domain"),
        P(None, "domain"),
    )
    return jax.shard_map(
        shards,
        mesh=mesh,
        in_specs=placed,
        out_specs=(P("band", "domain"), P("band", "domain"), P("band", "domain")),
        check_vma=False,
    )
```

```python
import jax
import jax.numpy as jnp
from jax import lax
from jax.sharding import PartitionSpec as P

DEGREE = 4


WEIGHTS = (
    -5369.0 / 1800.0,
    12.0 / 7.0,
    -15.0 / 56.0,
    10.0 / 189.0,
    -1.0 / 112.0,
    2.0 / 1925.0,
    -1.0 / 16632.0,
)
KINETIC = 50.0 / 9.0
CUT_SHARE = 0.1
SPECTRAL_REACH = (
    KINETIC
    * 3.0
    * (
        abs(WEIGHTS[0])
        + 2.0
        * (
            abs(WEIGHTS[1])
            + abs(WEIGHTS[2])
            + abs(WEIGHTS[3])
            + abs(WEIGHTS[4])
            + abs(WEIGHTS[5])
            + abs(WEIGHTS[6])
        )
    )
)


def dense(left, right):
    return lax.dot_general(
        left,
        right,
        (((1,), (0,)), ((), ())),
        precision=lax.Precision.HIGHEST,
        preferred_element_type=jnp.float32,
    )


def stencil_matrix(stencil, rows):
    slots = lax.broadcasted_iota(jnp.int32, (rows, stencil.shape[1]), 0)
    total = jnp.zeros((rows, stencil.shape[1]), jnp.float32)
    for distance in range(6):
        count = jnp.zeros((rows, stencil.shape[1]), jnp.float32)
        for member in range(6):
            count = count + (slots == stencil[6 * distance + member][None, :]).astype(jnp.float32)
        total = total + WEIGHTS[distance + 1] * count
    return total


def selection_matrix(send_list, live_slots, points):
    slots = lax.broadcasted_iota(jnp.int32, (points, send_list.shape[1]), 0)
    down = (slots == send_list[1][None, :]) & live_slots[1][None, :]
    up = (slots == send_list[0][None, :]) & live_slots[0][None, :]
    return jnp.concatenate([down, up], axis=1).astype(jnp.float32)


def apply_operator(values, potential, pick, near_local, near_below, near_above):
    capacity = pick.shape[1] // 2
    count = lax.axis_size("domain")
    outgoing = dense(values, pick)
    forward = [(i, (i + 1) % count) for i in range(count)]
    backward = [((i + 1) % count, i) for i in range(count)]
    from_below = lax.ppermute(outgoing[:, capacity:], "domain", forward)
    from_above = lax.ppermute(outgoing[:, :capacity], "domain", backward)
    near_sum = dense(values, near_local) + dense(from_above, near_above) + dense(from_below, near_below)
    return potential * values - KINETIC * (3.0 * WEIGHTS[0] * values + near_sum)


def filter_block(orbitals, operator_fn, lowest, highest):
    top_bound = highest + SPECTRAL_REACH
    cut_point = lowest + CUT_SHARE * (top_bound - lowest)
    half_width = (top_bound - cut_point) / 2.0
    centre = (top_bound + cut_point) / 2.0
    sigma_now = half_width / (lowest - centre)
    sigma_scale = 2.0 / sigma_now
    previous = orbitals
    current = sigma_now / half_width * (operator_fn(orbitals) - centre * orbitals)
    for order_index in range(2, DEGREE + 1):
        sigma_next = 1.0 / (sigma_scale - sigma_now)
        following = (
            2.0 * sigma_next / half_width * (operator_fn(current) - centre * current)
            - sigma_now * sigma_next * previous
        )
        previous = current
        current = following
        sigma_now = sigma_next
    return current


def inner_products(left_block, right_block):
    return lax.dot_general(
        left_block,
        right_block,
        (((1,), (1,)), ((), ())),
        precision=lax.Precision.HIGHEST,
        preferred_element_type=jnp.float32,
    )


def exchange(value, axis, step):
    count = lax.axis_size(axis)
    return lax.ppermute(value, axis, [(i, i ^ step) for i in range(count)])


def butterfly_max(value, axis):
    step = 1
    while step < lax.axis_size(axis):
        value = jnp.maximum(value, exchange(value, axis, step))
        step *= 2
    return value


def gather_blocks(block, axis, steps):
    index = lax.axis_index(axis)
    gathered = block
    for step in steps:
        received = exchange(gathered, axis, step)
        high = (index & step) != 0
        gathered = jnp.stack(
            [jnp.where(high, received, gathered), jnp.where(high, gathered, received)]
        )
    return gathered


def scatter_sum(parts, axis, steps):
    index = lax.axis_index(axis)
    current = parts
    for position, step in enumerate(steps):
        high = (index & step) != 0
        low_half = lax.index_in_dim(current, 0, axis=position + 1, keepdims=False)
        high_half = lax.index_in_dim(current, 1, axis=position + 1, keepdims=False)
        keep = jnp.where(high, high_half, low_half)
        send = jnp.where(high, low_half, high_half)
        current = keep + exchange(send, axis, step)
        current = jnp.expand_dims(current, position + 1)
    return current


def exchange_all(value, axis):
    count = lax.axis_size(axis)
    spread = jnp.broadcast_to(value[None], (count,) + value.shape)
    return lax.all_to_all(spread, axis, 0, 0, tiled=True)


def shards(orbitals, potential, stencil, send_list, send_count):
    rows, points = orbitals.shape
    capacity = send_list.shape[1]
    domain_count = lax.axis_size("domain")
    band_count = lax.axis_size("band")
    total_points = points * domain_count
    panel = exchange_all(orbitals, "band").reshape(band_count * rows, points)
    local_extremes = jnp.stack([-jnp.min(potential), jnp.max(potential)]) + 0.0 * panel[0, 0]
    extremes = jnp.max(exchange_all(local_extremes, "domain"), axis=0)
    lowest = -extremes[0]
    highest = extremes[1]
    live_slots = lax.broadcasted_iota(jnp.int32, (2, capacity), 1) < send_count

    pick = selection_matrix(send_list, live_slots, points)
    weight = stencil_matrix(stencil, points + 2 * capacity)
    near_local = weight[:points]
    near_below = weight[points : points + capacity]
    near_above = weight[points + capacity :]

    def operator_fn(values):
        return apply_operator(values, potential, pick, near_local, near_below, near_above)

    filtered_panel = filter_block(panel, operator_fn, lowest, highest)
    applied_panel = operator_fn(filtered_panel)
    band_index = lax.axis_index("band")
    filtered = lax.dynamic_slice_in_dim(filtered_panel, band_index * rows, rows, axis=0)
    parts = jnp.stack(
        [inner_products(filtered, filtered_panel), inner_products(filtered, applied_panel)]
    )
    blocks = jnp.transpose(parts.reshape(2, rows, domain_count, rows), (2, 0, 1, 3))
    sums = jnp.sum(lax.all_to_all(blocks, "domain", 0, 0, tiled=True), axis=0)
    return (filtered, sums[0] / total_points, sums[1] / total_points)


def solution(mesh):
    placed = (
        P("band", "domain"),
        P("domain"),
        P(None, "domain"),
        P(None, "domain"),
        P(None, "domain"),
    )
    return jax.shard_map(
        shards,
        mesh=mesh,
        in_specs=placed,
        out_specs=(P("band", "domain"), P("band", "domain"), P("band", "domain")),
        check_vma=False,
    )
```

```python
import jax
import jax.numpy as jnp
from jax import lax
from jax.sharding import PartitionSpec as P

DEGREE = 4


WEIGHTS = (
    -5369.0 / 1800.0,
    12.0 / 7.0,
    -15.0 / 56.0,
    10.0 / 189.0,
    -1.0 / 112.0,
    2.0 / 1925.0,
    -1.0 / 16632.0,
)
KINETIC = 50.0 / 9.0
CUT_SHARE = 0.1
SPECTRAL_REACH = (
    KINETIC
    * 3.0
    * (
        abs(WEIGHTS[0])
        + 2.0
        * (
            abs(WEIGHTS[1])
            + abs(WEIGHTS[2])
            + abs(WEIGHTS[3])
            + abs(WEIGHTS[4])
            + abs(WEIGHTS[5])
            + abs(WEIGHTS[6])
        )
    )
)


def dense(left, right):
    return lax.dot_general(
        left,
        right,
        (((1,), (0,)), ((), ())),
        precision=lax.Precision.HIGHEST,
        preferred_element_type=jnp.float32,
    )


def stencil_matrix(stencil, rows):
    slots = lax.broadcasted_iota(jnp.int32, (rows, stencil.shape[1]), 0)
    total = jnp.zeros((rows, stencil.shape[1]), jnp.float32)
    for distance in range(6):
        count = jnp.zeros((rows, stencil.shape[1]), jnp.float32)
        for member in range(6):
            count = count + (slots == stencil[6 * distance + member][None, :]).astype(jnp.float32)
        total = total + WEIGHTS[distance + 1] * count
    return total


def selection_matrix(send_list, live_slots, points):
    slots = lax.broadcasted_iota(jnp.int32, (points, send_list.shape[1]), 0)
    down = (slots == send_list[1][None, :]) & live_slots[1][None, :]
    up = (slots == send_list[0][None, :]) & live_slots[0][None, :]
    return jnp.concatenate([down, up], axis=1).astype(jnp.float32)


def select_columns(values, pick):
    high = lax.reduce_precision(values, exponent_bits=8, mantissa_bits=7)
    rest = values - high
    middle = lax.reduce_precision(rest, exponent_bits=8, mantissa_bits=7)
    low = rest - middle
    chosen = pick.astype(jnp.bfloat16)
    pieces = [
        lax.dot_general(
            piece.astype(jnp.bfloat16), chosen, (((1,), (0,)), ((), ())), preferred_element_type=jnp.float32
        )
        for piece in (high, middle, low)
    ]
    return pieces[0] + pieces[1] + pieces[2]


def apply_operator(values, potential, pick, near_local, near_below, near_above):
    capacity = pick.shape[1] // 2
    count = lax.axis_size("domain")
    outgoing = select_columns(values, pick)
    forward = [(i, (i + 1) % count) for i in range(count)]
    backward = [((i + 1) % count, i) for i in range(count)]
    from_below = lax.ppermute(outgoing[:, capacity:], "domain", forward)
    from_above = lax.ppermute(outgoing[:, :capacity], "domain", backward)
    near_sum = dense(values, near_local) + dense(from_above, near_above) + dense(from_below, near_below)
    return potential * values - KINETIC * (3.0 * WEIGHTS[0] * values + near_sum)


def filter_block(orbitals, operator_fn, lowest, highest):
    top_bound = highest + SPECTRAL_REACH
    cut_point = lowest + CUT_SHARE * (top_bound - lowest)
    half_width = (top_bound - cut_point) / 2.0
    centre = (top_bound + cut_point) / 2.0
    sigma_now = half_width / (lowest - centre)
    sigma_scale = 2.0 / sigma_now
    previous = orbitals
    current = sigma_now / half_width * (operator_fn(orbitals) - centre * orbitals)
    for order_index in range(2, DEGREE + 1):
        sigma_next = 1.0 / (sigma_scale - sigma_now)
        following = (
            2.0 * sigma_next / half_width * (operator_fn(current) - centre * current)
            - sigma_now * sigma_next * previous
        )
        previous = current
        current = following
        sigma_now = sigma_next
    return current


def inner_products(left_block, right_block):
    return lax.dot_general(
        left_block,
        right_block,
        (((1,), (1,)), ((), ())),
        precision=lax.Precision.HIGHEST,
        preferred_element_type=jnp.float32,
    )


def exchange(value, axis, step):
    count = lax.axis_size(axis)
    return lax.ppermute(value, axis, [(i, i ^ step) for i in range(count)])


def butterfly_max(value, axis):
    step = 1
    while step < lax.axis_size(axis):
        value = jnp.maximum(value, exchange(value, axis, step))
        step *= 2
    return value


def gather_blocks(block, axis, steps):
    index = lax.axis_index(axis)
    gathered = block
    for step in steps:
        received = exchange(gathered, axis, step)
        high = (index & step) != 0
        gathered = jnp.stack(
            [jnp.where(high, received, gathered), jnp.where(high, gathered, received)]
        )
    return gathered


def scatter_sum(parts, axis, steps):
    index = lax.axis_index(axis)
    current = parts
    for position, step in enumerate(steps):
        high = (index & step) != 0
        low_half = lax.index_in_dim(current, 0, axis=position + 1, keepdims=False)
        high_half = lax.index_in_dim(current, 1, axis=position + 1, keepdims=False)
        keep = jnp.where(high, high_half, low_half)
        send = jnp.where(high, low_half, high_half)
        current = keep + exchange(send, axis, step)
        current = jnp.expand_dims(current, position + 1)
    return current


def exchange_all(value, axis):
    count = lax.axis_size(axis)
    spread = jnp.broadcast_to(value[None], (count,) + value.shape)
    return lax.all_to_all(spread, axis, 0, 0, tiled=True)


def shards(orbitals, potential, stencil, send_list, send_count):
    rows, points = orbitals.shape
    capacity = send_list.shape[1]
    domain_count = lax.axis_size("domain")
    band_count = lax.axis_size("band")
    total_points = points * domain_count
    panel = exchange_all(orbitals, "band").reshape(band_count * rows, points)
    local_extremes = jnp.stack([-jnp.min(potential), jnp.max(potential)])
    extremes = jnp.max(exchange_all(local_extremes, "domain"), axis=0)
    lowest = -extremes[0]
    highest = extremes[1]
    live_slots = lax.broadcasted_iota(jnp.int32, (2, capacity), 1) < send_count

    pick = selection_matrix(send_list, live_slots, points)
    weight = stencil_matrix(stencil, points + 2 * capacity)
    near_local = weight[:points]
    near_below = weight[points : points + capacity]
    near_above = weight[points + capacity :]

    def operator_fn(values):
        return apply_operator(values, potential, pick, near_local, near_below, near_above)

    filtered_panel = filter_block(panel, operator_fn, lowest, highest)
    applied_panel = operator_fn(filtered_panel)
    band_index = lax.axis_index("band")
    filtered = lax.dynamic_slice_in_dim(filtered_panel, band_index * rows, rows, axis=0)
    parts = jnp.stack(
        [inner_products(filtered, filtered_panel), inner_products(filtered, applied_panel)]
    )
    blocks = jnp.transpose(parts.reshape(2, rows, domain_count, rows), (2, 0, 1, 3))
    sums = jnp.sum(lax.all_to_all(blocks, "domain", 0, 0, tiled=True), axis=0)
    return (filtered, sums[0] / total_points, sums[1] / total_points)


def solution(mesh):
    placed = (
        P("band", "domain"),
        P("domain"),
        P(None, "domain"),
        P(None, "domain"),
        P(None, "domain"),
    )
    return jax.shard_map(
        shards,
        mesh=mesh,
        in_specs=placed,
        out_specs=(P("band", "domain"), P("band", "domain"), P("band", "domain")),
        check_vma=False,
    )
```
